512 devices in a mesh: tm: 16 (over x_lo, y, core), chan: 32 (over z, x_hi).
Axes of the slice: x: 4 (x_hi: 2, x_lo: 2; x = x_hi * 2 + x_lo), y: 4, z: 16, core: 2. Of those that a mesh axis runs over, the one named last changes fastest.
Arguments:
- record: bfloat16 [16384, 16384], P('chan', 'tm'), may hold values from -120 to 120, as said below
- band_taper: float32 [256], replicated, may hold values from 0.25 to 2
- src_offset: int32 [2, 64], replicated, may hold values from 0 to 511
Outputs:
- correlation: bfloat16 [128, 16384, 256], P(None, ('chan', 'tm'))
The draws below stay inside these ranges and needn't reach their ends.
Inputs may be any that keep to these rules, and one draw needn't show every extreme that they name: `record`: real-valued samples.
All inputs are finite; a program needn't handle non-finite values.
Results may differ from the reference program's by a relative error of at most 0.0085.
Values may be sent and summed in bfloat16 or wider, within the bound.
No kernel may reach another device: no remote copies, remote signals or barrier semaphores. Data moves between devices by JAX's collectives and lax.ppermute only.
A program may use at most 64 MiB of HBM per device.

```python
import math
import jax
import jax.numpy as jnp
from jax import lax

SAMP = 1024
NF = 256
LOW_BIN = 32
LAGS = 256
SRC_BLK = 2
ROUNDS = 2
BLOCK = 512
CH = 16384
SEGS = 16
SRC = 64


def draw_record(key, part):
    noise_key = jax.random.fold_in(key, 11)
    scale_key = jax.random.fold_in(key, 12)
    noise_raw = jnp.clip(jax.random.normal(noise_key, (CH, SEGS * SAMP), jnp.float32), -6.0, 6.0)
    colour = 0.95
    scales = jnp.exp(jax.random.uniform(scale_key, (CH, 1), jnp.float32, 0.0, 1.0) * math.log(10.0))
    coloured = noise_raw + colour * jnp.roll(noise_raw, 1, axis=1)
    return (scales * coloured).astype(jnp.bfloat16)


def place_ends(drawn, stream_key, smallest, top_value):
    place = [jax.random.randint(jax.random.fold_in(stream_key, axis), (), 0, length) for axis, length in enumerate(drawn.shape)]
    main_axis = drawn.shape.index(max(drawn.shape))
    neighbour = place[:main_axis] + [(place[main_axis] + 1) % drawn.shape[main_axis]] + place[main_axis + 1:]
    return drawn.at[tuple(place)].set(smallest).at[tuple(neighbour)].set(top_value)


def setup_inputs(seed: int = 0) -> dict:
    key_of = jax.random.split(jax.random.key(seed), 4)
    record = draw_record(jax.random.fold_in(key_of[3], 71), 0)
    band_taper = jnp.clip(jnp.exp(jax.random.uniform(key_of[1], (NF,), jnp.float32, math.log(0.25), math.log(2.0))), 0.25, 2.0)
    src_offset = place_ends(jax.random.randint(key_of[2], (ROUNDS, SRC), 0, BLOCK), jax.random.fold_in(key_of[2], 1), 0, BLOCK - 1).astype(jnp.int32)
    return {"record": record, "band_taper": band_taper, "src_offset": src_offset}


def make_tables(sample_count, bin_count, low_bin, lag_count):
    sample_index = jnp.arange(sample_count, dtype=jnp.int32)
    bin_index = low_bin + jnp.arange(bin_count, dtype=jnp.int32)
    angles = (sample_index[:, None] * bin_index[None, :] % sample_count).astype(jnp.float32) * (2.0 * math.pi / sample_count)
    dft_table = jnp.concatenate([jnp.cos(angles), -jnp.sin(angles)], 1).astype(jnp.bfloat16)
    lag_shift = jnp.arange(lag_count, dtype=jnp.int32) - lag_count // 2 + sample_count
    lag_angles = (bin_index[:, None] * lag_shift[None, :] % sample_count).astype(jnp.float32) * (2.0 * math.pi / sample_count)
    lag_table = jnp.concatenate([jnp.cos(lag_angles), -jnp.sin(lag_angles)], 0).astype(jnp.bfloat16)
    return (dft_table, lag_table)

def whiten(spectrum, band_taper):
    bin_count = band_taper.shape[0]
    re_part = spectrum[..., :bin_count]
    im_part = spectrum[..., bin_count:]
    bin_power = re_part * re_part + im_part * im_part
    mean_power = lax.optimization_barrier(jnp.mean(bin_power, axis=-1, keepdims=True))
    divisor = jnp.sqrt(bin_power + 0.5 * mean_power + 1e-06)
    gain_row = band_taper / divisor
    return jnp.concatenate([re_part * gain_row, im_part * gain_row], -1).astype(jnp.bfloat16)

def reference(record, band_taper, src_offset):
    dft_table, lag_table = make_tables(SAMP, NF, LOW_BIN, LAGS)
    segments = jnp.transpose(record.reshape(CH, SEGS, SAMP), (1, 0, 2))

    def transform(segment_rows):
        spectrum = jnp.dot(segment_rows.astype(jnp.float32), dft_table.astype(jnp.float32), precision=lax.Precision.HIGHEST)
        return whiten(spectrum, band_taper)
    whitened = lax.map(transform, segments)
    recv_real = whitened[..., :NF].astype(jnp.float32)
    recv_imag = whitened[..., NF:].astype(jnp.float32)
    norm_scale = 1.0 / math.sqrt(NF * SEGS)
    highest = lax.Precision.HIGHEST

    def per_source(source_row):
        src_real = source_row[:, :NF].astype(jnp.float32)
        src_imag = source_row[:, NF:].astype(jnp.float32)
        real_part = jnp.einsum('gj,gcj->cj', src_real, recv_real, precision=highest) + jnp.einsum('gj,gcj->cj', src_imag, recv_imag, precision=highest)
        imag_part = jnp.einsum('gj,gcj->cj', src_imag, recv_real, precision=highest) - jnp.einsum('gj,gcj->cj', src_real, recv_imag, precision=highest)
        stacked = jnp.concatenate([real_part, imag_part], -1).astype(jnp.bfloat16)
        lagged = jnp.dot(stacked, lag_table, preferred_element_type=jnp.float32)
        return (lagged * norm_scale).astype(jnp.bfloat16)
    results = []
    for round_index in range(ROUNDS):
        source_chan = jnp.arange(SRC, dtype=jnp.int32) // SRC_BLK * BLOCK + src_offset[round_index].astype(jnp.int32)
        sources = jnp.transpose(whitened[:, source_chan, :], (1, 0, 2))
        results.append(lax.map(per_source, sources))
    return jnp.concatenate(results, 0)
```

```python
import math

import jax
import jax.numpy as jnp
from jax import lax
from jax.sharding import PartitionSpec as P

LOW_BIN = 32
LAGS = 256
SRC_BLK = 2
ROUNDS = 2


def make_tables(sample_count, bin_count, low_bin, lag_count):
    sample_index = jnp.arange(sample_count, dtype=jnp.int32)
    bin_index = low_bin + jnp.arange(bin_count, dtype=jnp.int32)
    angles = (sample_index[:, None] * bin_index[None, :] % sample_count).astype(jnp.float32) * (
        2.0 * math.pi / sample_count
    )
    dft_table = jnp.concatenate([jnp.cos(angles), -jnp.sin(angles)], 1).astype(jnp.bfloat16)
    lag_shift = jnp.arange(lag_count, dtype=jnp.int32) - lag_count // 2 + sample_count
    lag_angles = (bin_index[:, None] * lag_shift[None, :] % sample_count).astype(jnp.float32) * (
        2.0 * math.pi / sample_count
    )
    lag_table = jnp.concatenate([jnp.cos(lag_angles), -jnp.sin(lag_angles)], 0).astype(jnp.bfloat16)
    return (dft_table, lag_table)


def whiten(spectrum, band_taper):
    bin_count = band_taper.shape[0]
    re_part = spectrum[..., :bin_count]
    im_part = spectrum[..., bin_count:]
    bin_power = re_part * re_part + im_part * im_part
    mean_power = jnp.mean(bin_power, axis=-1, keepdims=True)
    divisor = jnp.sqrt(bin_power + 0.5 * mean_power + 1e-06)
    gain_row = band_taper / divisor
    return jnp.concatenate([re_part * gain_row, im_part * gain_row], -1).astype(jnp.bfloat16)


def gather_over(piece, axis):
    count = lax.axis_size(axis)
    copies = jnp.broadcast_to(piece[None], (count,) + piece.shape)
    return lax.all_to_all(copies, axis, 0, 0, tiled=False)


def share_sources(picked):
    by_block = gather_over(picked, "chan")
    return gather_over(by_block, "tm")


def correlate(sources, receivers, lag_table, norm_scale):
    bin_count = sources.shape[2] // 2
    src_real = sources[..., :bin_count]
    src_imag = sources[..., bin_count:]
    recv_real = receivers[..., :bin_count]
    recv_imag = receivers[..., bin_count:]
    real_part = jnp.einsum(
        "gsj,grj->srj", src_real, recv_real, preferred_element_type=jnp.float32
    ) + jnp.einsum("gsj,grj->srj", src_imag, recv_imag, preferred_element_type=jnp.float32)
    imag_part = jnp.einsum(
        "gsj,grj->srj", src_imag, recv_real, preferred_element_type=jnp.float32
    ) - jnp.einsum("gsj,grj->srj", src_real, recv_imag, preferred_element_type=jnp.float32)
    stacked = jnp.concatenate([real_part, imag_part], -1).astype(jnp.bfloat16)
    lagged = jnp.einsum("srf,fl->srl", stacked, lag_table, preferred_element_type=jnp.float32)
    return (lagged * norm_scale).astype(jnp.bfloat16)


def local(record, band_taper, src_offset):
    block_rows = record.shape[0]
    sample_count = record.shape[1]
    bin_count = band_taper.shape[0]
    dft_table, lag_table = make_tables(sample_count, bin_count, LOW_BIN, LAGS)
    spectrum = jnp.dot(record, dft_table, preferred_element_type=jnp.float32)
    whitened = whiten(spectrum, band_taper)
    chan_index = lax.axis_index("chan")
    offsets = lax.dynamic_slice_in_dim(src_offset, chan_index * SRC_BLK, SRC_BLK, 1)
    onehot = (offsets[:, :, None] == jnp.arange(block_rows, dtype=jnp.int32)[None, None, :]).astype(
        jnp.bfloat16
    )
    picked = jnp.einsum("rsb,bf->rsf", onehot, whitened, preferred_element_type=jnp.float32).astype(
        jnp.bfloat16
    )
    feat = picked.shape[-1]
    shared = share_sources(picked.reshape(ROUNDS * SRC_BLK, feat))
    segs, blocks = shared.shape[0], shared.shape[1]
    shared = shared.reshape(segs, blocks, ROUNDS, SRC_BLK, feat)
    receivers = lax.all_to_all(whitened[None], "tm", split_axis=1, concat_axis=0, tiled=True)
    segments = receivers.shape[0]
    norm_scale = 1.0 / math.sqrt(bin_count * segments)
    results = []
    for round_index in range(ROUNDS):
        round_sources = shared[:, :, round_index].reshape(segs, blocks * SRC_BLK, feat)
        results.append(correlate(round_sources, receivers, lag_table, norm_scale))
    return jnp.concatenate(results, 0)


def solution(mesh):
    in_specs = (P("chan", "tm"), P(), P())
    out_specs = P(None, ("chan", "tm"), None)
    return jax.shard_map(local, mesh=mesh, in_specs=in_specs, out_specs=out_specs, check_vma=False)
```

```python
import math

import jax
import jax.numpy as jnp
from jax import lax
from jax.sharding import PartitionSpec as P

LOW_BIN = 32
LAGS = 256
SRC_BLK = 2
ROUNDS = 2


def make_tables(sample_count, bin_count, low_bin, lag_count):
    sample_index = jnp.arange(sample_count, dtype=jnp.int32)
    bin_index = low_bin + jnp.arange(bin_count, dtype=jnp.int32)
    angles = (sample_index[:, None] * bin_index[None, :] % sample_count).astype(jnp.float32) * (
        2.0 * math.pi / sample_count
    )
    dft_table = jnp.concatenate([jnp.cos(angles), -jnp.sin(angles)], 1).astype(jnp.bfloat16)
    lag_shift = jnp.arange(lag_count, dtype=jnp.int32) - lag_count // 2 + sample_count
    lag_angles = (bin_index[:, None] * lag_shift[None, :] % sample_count).astype(jnp.float32) * (
        2.0 * math.pi / sample_count
    )
    lag_table = jnp.concatenate([jnp.cos(lag_angles), -jnp.sin(lag_angles)], 0).astype(jnp.bfloat16)
    return (dft_table, lag_table)


def whiten(spectrum, band_taper):
    bin_count = band_taper.shape[0]
    re_part = spectrum[..., :bin_count]
    im_part = spectrum[..., bin_count:]
    bin_power = re_part * re_part + im_part * im_part
    mean_power = jnp.mean(bin_power, axis=-1, keepdims=True)
    divisor = jnp.sqrt(bin_power + 0.5 * mean_power + 1e-06)
    gain_row = band_taper / divisor
    return jnp.concatenate([re_part * gain_row, im_part * gain_row], -1).astype(jnp.bfloat16)


def gather_over(piece, axis):
    count = lax.axis_size(axis)
    copies = jnp.broadcast_to(piece[None], (count,) + piece.shape)
    return lax.all_to_all(copies, axis, 0, 0, tiled=False)


def correlate(sources, receivers, lag_table, norm_scale):
    bin_count = sources.shape[2] // 2
    src_real = sources[..., :bin_count]
    src_imag = sources[..., bin_count:]
    recv_real = receivers[..., :bin_count]
    recv_imag = receivers[..., bin_count:]
    real_part = jnp.einsum(
        "gsj,grj->srj", src_real, recv_real, preferred_element_type=jnp.float32
    ) + jnp.einsum("gsj,grj->srj", src_imag, recv_imag, preferred_element_type=jnp.float32)
    imag_part = jnp.einsum(
        "gsj,grj->srj", src_imag, recv_real, preferred_element_type=jnp.float32
    ) - jnp.einsum("gsj,grj->srj", src_real, recv_imag, preferred_element_type=jnp.float32)
    stacked = jnp.concatenate([real_part, imag_part], -1).astype(jnp.bfloat16)
    lagged = jnp.einsum("srf,fl->srl", stacked, lag_table, preferred_element_type=jnp.float32)
    return (lagged * norm_scale).astype(jnp.bfloat16)


def local(record, band_taper, src_offset):
    block_rows = record.shape[0]
    sample_count = record.shape[1]
    bin_count = band_taper.shape[0]
    dft_table, lag_table = make_tables(sample_count, bin_count, LOW_BIN, LAGS)
    spectrum = jnp.dot(record, dft_table, preferred_element_type=jnp.float32)
    whitened = whiten(spectrum, band_taper)
    chan_index = lax.axis_index("chan")
    offsets = lax.dynamic_slice_in_dim(src_offset, chan_index * SRC_BLK, SRC_BLK, 1)
    onehot = (offsets[:, :, None] == jnp.arange(block_rows, dtype=jnp.int32)[None, None, :]).astype(
        jnp.bfloat16
    )
    picked = jnp.einsum("rsb,bf->rsf", onehot, whitened, preferred_element_type=jnp.float32).astype(
        jnp.bfloat16
    )
    feat = picked.shape[-1]
    by_block = gather_over(picked.reshape(ROUNDS * SRC_BLK, feat), "chan")
    blocks = by_block.shape[0]
    tm_count = lax.axis_size("tm")
    to_send = jnp.concatenate(
        [
            whitened.reshape(tm_count, block_rows // tm_count, feat),
            jnp.broadcast_to(by_block.reshape(1, -1, feat), (tm_count, blocks * ROUNDS * SRC_BLK, feat)),
        ],
        1,
    )
    arrived = lax.all_to_all(to_send, "tm", 0, 0, tiled=False)
    receivers = arrived[:, : block_rows // tm_count]
    segs = arrived.shape[0]
    shared = arrived[:, block_rows // tm_count :].reshape(segs, blocks, ROUNDS, SRC_BLK, feat)
    segments = receivers.shape[0]
    norm_scale = 1.0 / math.sqrt(bin_count * segments)
    results = []
    for round_index in range(ROUNDS):
        round_sources = shared[:, :, round_index].reshape(segs, blocks * SRC_BLK, feat)
        results.append(correlate(round_sources, receivers, lag_table, norm_scale))
    return jnp.concatenate(results, 0)


def solution(mesh):
    in_specs = (P("chan", "tm"), P(), P())
    out_specs = P(None, ("chan", "tm"), None)
    return jax.shard_map(local, mesh=mesh, in_specs=in_specs, out_specs=out_specs, check_vma=False)
```

```python
import functools
import math

import jax
import jax.numpy as jnp
from jax import lax
from jax.experimental import pallas as pl
from jax.experimental.pallas import tpu as pltpu
from jax.sharding import PartitionSpec as P

LOW_BIN = 32
LAGS = 256
SRC_BLK = 2
ROUNDS = 2


def make_tables(sample_count, bin_count, low_bin, lag_count):
    sample_index = jnp.arange(sample_count, dtype=jnp.int32)
    bin_index = low_bin + jnp.arange(bin_count, dtype=jnp.int32)
    angles = (sample_index[:, None] * bin_index[None, :] % sample_count).astype(jnp.float32) * (
        2.0 * math.pi / sample_count
    )
    dft_table = jnp.concatenate([jnp.cos(angles), -jnp.sin(angles)], 1).astype(jnp.bfloat16)
    lag_shift = jnp.arange(lag_count, dtype=jnp.int32) - lag_count // 2 + sample_count
    lag_angles = (bin_index[:, None] * lag_shift[None, :] % sample_count).astype(jnp.float32) * (
        2.0 * math.pi / sample_count
    )
    lag_table = jnp.concatenate([jnp.cos(lag_angles), -jnp.sin(lag_angles)], 0).astype(jnp.bfloat16)
    return (dft_table, lag_table)


def whiten(spectrum, band_taper):
    bin_count = band_taper.shape[0]
    re_part = spectrum[..., :bin_count]
    im_part = spectrum[..., bin_count:]
    bin_power = re_part * re_part + im_part * im_part
    mean_power = jnp.mean(bin_power, axis=-1, keepdims=True)
    divisor = jnp.sqrt(bin_power + 0.5 * mean_power + 1e-06)
    gain_row = band_taper / divisor
    return jnp.concatenate([re_part * gain_row, im_part * gain_row], -1).astype(jnp.bfloat16)


def gather_over(piece, axis):
    count = lax.axis_size(axis)
    copies = jnp.broadcast_to(piece[None], (count,) + piece.shape)
    return lax.all_to_all(copies, axis, 0, 0, tiled=False)


def share_sources(picked):
    by_block = gather_over(picked, "chan")
    return gather_over(by_block, "tm")


def correlate_kernel(src_ref, p_ref, q_ref, r_ref, lag_ref, out_ref, stk_ref, *, norm, per):
    block, segs, _ = src_ref.shape
    chans, bins = p_ref.shape[1], p_ref.shape[2]

    def body(k, carry):
        acc = [[jnp.zeros((chans, bins), jnp.float32) for _ in range(3)] for _ in range(per)]
        for g in range(segs):
            pg, qg, rg = p_ref[g], q_ref[g], r_ref[g]
            for u in range(per):
                row = src_ref[k * per + u, pl.ds(g, 1), :]
                a_re, a_im = row[:, :bins], row[:, bins:]
                acc[u][0] = acc[u][0] + pg * (a_re + a_im)
                acc[u][1] = acc[u][1] + qg * a_re
                acc[u][2] = acc[u][2] + rg * a_im
        for u in range(per):
            start = pl.multiple_of((k * per + u) * chans, chans)
            stk_ref[pl.ds(start, chans), :bins] = (acc[u][0] - acc[u][2]).astype(stk_ref.dtype)
            stk_ref[pl.ds(start, chans), bins:] = (acc[u][0] + acc[u][1]).astype(stk_ref.dtype)
        return carry

    lax.fori_loop(0, block // per, body, 0)
    lagged = jnp.dot(stk_ref[...], lag_ref[...], preferred_element_type=jnp.float32)
    out_ref[...] = (lagged * norm).astype(out_ref.dtype).reshape(out_ref.shape)


def correlate(sources, receivers, lag_table, norm_scale, block=32, per=2):
    n_src, segs, feat = sources.shape
    chans = receivers.shape[1]
    bins = feat // 2
    lags = lag_table.shape[1]
    b_re = receivers[..., :bins].astype(jnp.float32)
    b_im = receivers[..., bins:].astype(jnp.float32)
    recv_p, recv_q, recv_r = b_re, -b_im - b_re, b_re - b_im
    recv_spec = pl.BlockSpec((segs, chans, bins), lambda i: (0, 0, 0))
    return pl.pallas_call(
        functools.partial(correlate_kernel, norm=norm_scale, per=per),
        grid=(n_src // block,),
        in_specs=[
            pl.BlockSpec((block, segs, feat), lambda i: (i, 0, 0)),
            recv_spec,
            recv_spec,
            recv_spec,
            pl.BlockSpec((feat, lags), lambda i: (0, 0)),
        ],
        out_specs=pl.BlockSpec((block, chans, lags), lambda i: (i, 0, 0)),
        out_shape=jax.ShapeDtypeStruct((n_src, chans, lags), jnp.bfloat16),
        scratch_shapes=[pltpu.VMEM((block * chans, feat), jnp.bfloat16)],
    )(sources.astype(jnp.float32), recv_p, recv_q, recv_r, lag_table)


def local(record, band_taper, src_offset):
    block_rows = record.shape[0]
    sample_count = record.shape[1]
    bin_count = band_taper.shape[0]
    dft_table, lag_table = make_tables(sample_count, bin_count, LOW_BIN, LAGS)
    spectrum = jnp.dot(record, dft_table, preferred_element_type=jnp.float32)
    whitened = whiten(spectrum, band_taper)
    chan_index = lax.axis_index("chan")
    offsets = lax.dynamic_slice_in_dim(src_offset, chan_index * SRC_BLK, SRC_BLK, 1)
    onehot = (offsets[:, :, None] == jnp.arange(block_rows, dtype=jnp.int32)[None, None, :]).astype(
        jnp.bfloat16
    )
    picked = jnp.einsum("rsb,bf->rsf", onehot, whitened, preferred_element_type=jnp.float32).astype(
        jnp.bfloat16
    )
    feat = picked.shape[-1]
    shared = share_sources(picked.reshape(ROUNDS * SRC_BLK, feat))
    receivers = lax.all_to_all(whitened[None], "tm", split_axis=1, concat_axis=0, tiled=True)
    segments = receivers.shape[0]
    norm_scale = 1.0 / math.sqrt(bin_count * segments)
    segs, blocks = shared.shape[0], shared.shape[1]
    ordered = jnp.transpose(shared.reshape(segs, blocks, ROUNDS, SRC_BLK, feat), (2, 1, 3, 0, 4))
    ordered = ordered.reshape(ROUNDS * blocks * SRC_BLK, segs, feat)
    return correlate(ordered, receivers, lag_table, norm_scale)


def solution(mesh):
    in_specs = (P("chan", "tm"), P(), P())
    out_specs = P(None, ("chan", "tm"), None)
    return jax.shard_map(local, mesh=mesh, in_specs=in_specs, out_specs=out_specs, check_vma=False)
```

```python
import functools
import math

import jax
import ml_dtypes
import numpy as np
import jax.numpy as jnp
from jax import lax
from jax.experimental import pallas as pl
from jax.experimental.pallas import tpu as pltpu
from jax.sharding import PartitionSpec as P

LOW_BIN = 32
LAGS = 256
SRC_BLK = 2
ROUNDS = 2


def make_tables(sample_count, bin_count, low_bin, lag_count):
    sample_index = jnp.arange(sample_count, dtype=jnp.int32)
    bin_index = low_bin + jnp.arange(bin_count, dtype=jnp.int32)
    angles = (sample_index[:, None] * bin_index[None, :] % sample_count).astype(jnp.float32) * (
        2.0 * math.pi / sample_count
    )
    dft_table = jnp.concatenate([jnp.cos(angles), -jnp.sin(angles)], 1).astype(jnp.bfloat16)
    lag_shift = jnp.arange(lag_count, dtype=jnp.int32) - lag_count // 2 + sample_count
    lag_angles = (bin_index[:, None] * lag_shift[None, :] % sample_count).astype(jnp.float32) * (
        2.0 * math.pi / sample_count
    )
    lag_table = jnp.concatenate([jnp.cos(lag_angles), -jnp.sin(lag_angles)], 0).astype(jnp.bfloat16)
    return (dft_table, lag_table)


def const_tables(sample_count, bin_count, low_bin, lag_count):
    sample_index = np.arange(sample_count, dtype=np.int64)
    bin_index = low_bin + np.arange(bin_count, dtype=np.int64)
    step = np.float32(2.0 * math.pi / sample_count)
    angles = (sample_index[:, None] * bin_index[None, :] % sample_count).astype(np.float32) * step
    dft_table = np.concatenate([np.cos(angles), -np.sin(angles)], 1).astype(ml_dtypes.bfloat16)
    lag_shift = np.arange(lag_count, dtype=np.int64) - lag_count // 2 + sample_count
    lag_angles = (bin_index[:, None] * lag_shift[None, :] % sample_count).astype(np.float32) * step
    lag_table = np.concatenate([np.cos(lag_angles), -np.sin(lag_angles)], 0).astype(ml_dtypes.bfloat16)
    return (jnp.asarray(dft_table), jnp.asarray(lag_table))


def whiten(spectrum, band_taper):
    bin_count = band_taper.shape[0]
    re_part = spectrum[..., :bin_count]
    im_part = spectrum[..., bin_count:]
    bin_power = re_part * re_part + im_part * im_part
    mean_power = jnp.mean(bin_power, axis=-1, keepdims=True)
    divisor = jnp.sqrt(bin_power + 0.5 * mean_power + 1e-06)
    gain_row = band_taper / divisor
    return jnp.concatenate([re_part * gain_row, im_part * gain_row], -1).astype(jnp.bfloat16)


def gather_over(piece, axis):
    count = lax.axis_size(axis)
    copies = jnp.broadcast_to(piece[None], (count,) + piece.shape)
    return lax.all_to_all(copies, axis, 0, 0, tiled=False)


def share_sources(picked):
    by_block = gather_over(picked, "chan")
    return gather_over(by_block, "tm")


def correlate_kernel(recv_ref, src_ref, lag_ref, out_ref, src_sc, p_sc, q_sc, r_sc, stk_ref, *, norm, recv_off, src_off):
    segs, chans, bins = p_sc.shape
    n_src = src_sc.shape[1]
    block = out_ref.shape[0]
    step = pl.program_id(0)

    @pl.when(step == 0)
    def _():
        for g in range(segs):
            rec = recv_ref[g, recv_off : recv_off + chans, :].astype(jnp.float32)
            b_re, b_im = rec[:, :bins], rec[:, bins:]
            p_sc[g] = b_re
            q_sc[g] = -b_im - b_re
            r_sc[g] = b_re - b_im
            src_sc[g] = src_ref[g, src_off : src_off + n_src, :].astype(jnp.float32)

    per_round = n_src // ROUNDS
    steps_per_round = per_round // block
    rnd = step // steps_per_round
    first_blk = (step % steps_per_round) * (block // SRC_BLK)

    def body(k, carry):
        acc = [[jnp.zeros((chans, bins), jnp.float32) for _ in range(3)] for _ in range(SRC_BLK)]
        base = (first_blk + k) * (ROUNDS * SRC_BLK) + rnd * SRC_BLK
        for g in range(segs):
            pg, qg, rg = p_sc[g], q_sc[g], r_sc[g]
            for u in range(SRC_BLK):
                row = src_sc[g, pl.ds(base + u, 1), :]
                a_re, a_im = row[:, :bins], row[:, bins:]
                acc[u][0] = acc[u][0] + pg * (a_re + a_im)
                acc[u][1] = acc[u][1] + qg * a_re
                acc[u][2] = acc[u][2] + rg * a_im
        for u in range(SRC_BLK):
            start = pl.multiple_of((k * SRC_BLK + u) * chans, chans)
            stk_ref[pl.ds(start, chans), :bins] = (acc[u][0] - acc[u][2]).astype(stk_ref.dtype)
            stk_ref[pl.ds(start, chans), bins:] = (acc[u][0] + acc[u][1]).astype(stk_ref.dtype)
        return carry

    lax.fori_loop(0, block // SRC_BLK, body, 0)
    lagged = jnp.dot(stk_ref[...], lag_ref[...], preferred_element_type=jnp.float32)
    out_ref[...] = (lagged * norm).astype(out_ref.dtype).reshape(out_ref.shape)


def correlate(recv_arr, recv_off, chans, src_arr, src_off, n_src, lag_table, norm_scale, block=32):
    segs, _, feat = src_arr.shape
    bins = feat // 2
    lags = lag_table.shape[1]
    return pl.pallas_call(
        functools.partial(correlate_kernel, norm=norm_scale, recv_off=recv_off, src_off=src_off),
        grid=(n_src // block,),
        in_specs=[
            pl.BlockSpec(recv_arr.shape, lambda i: (0, 0, 0)),
            pl.BlockSpec(src_arr.shape, lambda i: (0, 0, 0)),
            pl.BlockSpec((feat, lags), lambda i: (0, 0)),
        ],
        out_specs=pl.BlockSpec((block, chans, lags), lambda i: (i, 0, 0)),
        out_shape=jax.ShapeDtypeStruct((n_src, chans, lags), jnp.bfloat16),
        scratch_shapes=[
            pltpu.VMEM((segs, n_src, feat), jnp.float32),
            pltpu.VMEM((segs, chans, bins), jnp.float32),
            pltpu.VMEM((segs, chans, bins), jnp.float32),
            pltpu.VMEM((segs, chans, bins), jnp.float32),
            pltpu.VMEM((block * chans, feat), jnp.bfloat16),
        ],
        compiler_params=pltpu.CompilerParams(
            dimension_semantics=("arbitrary",), vmem_limit_bytes=48 * 1024 * 1024
        ),
    )(recv_arr, src_arr, lag_table)


def local(record, band_taper, src_offset):
    block_rows = record.shape[0]
    sample_count = record.shape[1]
    bin_count = band_taper.shape[0]
    dft_table, lag_table = const_tables(sample_count, bin_count, LOW_BIN, LAGS)
    spectrum = jnp.dot(record, dft_table, preferred_element_type=jnp.float32)
    whitened = whiten(spectrum, band_taper)
    chan_index = lax.axis_index("chan")
    offsets = lax.dynamic_slice_in_dim(src_offset, chan_index * SRC_BLK, SRC_BLK, 1)
    onehot = (offsets[:, :, None] == jnp.arange(block_rows, dtype=jnp.int32)[None, None, :]).astype(
        jnp.bfloat16
    )
    picked = jnp.einsum("rsb,bf->rsf", onehot, whitened, preferred_element_type=jnp.float32).astype(
        jnp.bfloat16
    )
    feat = picked.shape[-1]
    by_block = gather_over(picked.reshape(ROUNDS * SRC_BLK, feat), "chan")
    blocks = by_block.shape[0]
    tm_count = lax.axis_size("tm")
    to_send = jnp.concatenate(
        [
            whitened.reshape(tm_count, block_rows // tm_count, feat),
            jnp.broadcast_to(by_block.reshape(1, -1, feat), (tm_count, blocks * ROUNDS * SRC_BLK, feat)),
        ],
        1,
    )
    arrived = lax.all_to_all(to_send, "tm", 0, 0, tiled=False)
    chans = block_rows // tm_count
    n_src = blocks * ROUNDS * SRC_BLK
    norm_scale = 1.0 / math.sqrt(bin_count * tm_count)
    return correlate(arrived, 0, chans, arrived, chans, n_src, lag_table, norm_scale)


def solution(mesh):
    in_specs = (P("chan", "tm"), P(), P())
    out_specs = P(None, ("chan", "tm"), None)
    return jax.shard_map(local, mesh=mesh, in_specs=in_specs, out_specs=out_specs, check_vma=False)
```

```python
import functools
import math

import jax
import ml_dtypes
import numpy as np
import jax.numpy as jnp
from jax import lax
from jax.experimental import pallas as pl
from jax.experimental.pallas import tpu as pltpu
from jax.sharding import PartitionSpec as P

LOW_BIN = 32
LAGS = 256
SRC_BLK = 2
ROUNDS = 2


def make_tables(sample_count, bin_count, low_bin, lag_count):
    sample_index = jnp.arange(sample_count, dtype=jnp.int32)
    bin_index = low_bin + jnp.arange(bin_count, dtype=jnp.int32)
    angles = (sample_index[:, None] * bin_index[None, :] % sample_count).astype(jnp.float32) * (
        2.0 * math.pi / sample_count
    )
    dft_table = jnp.concatenate([jnp.cos(angles), -jnp.sin(angles)], 1).astype(jnp.bfloat16)
    lag_shift = jnp.arange(lag_count, dtype=jnp.int32) - lag_count // 2 + sample_count
    lag_angles = (bin_index[:, None] * lag_shift[None, :] % sample_count).astype(jnp.float32) * (
        2.0 * math.pi / sample_count
    )
    lag_table = jnp.concatenate([jnp.cos(lag_angles), -jnp.sin(lag_angles)], 0).astype(jnp.bfloat16)
    return (dft_table, lag_table)


def const_tables(sample_count, bin_count, low_bin, lag_count):
    sample_index = np.arange(sample_count, dtype=np.int64)
    bin_index = low_bin + np.arange(bin_count, dtype=np.int64)
    step = np.float32(2.0 * math.pi / sample_count)
    angles = (sample_index[:, None] * bin_index[None, :] % sample_count).astype(np.float32) * step
    dft_table = np.concatenate([np.cos(angles), -np.sin(angles)], 1).astype(ml_dtypes.bfloat16)
    lag_shift = np.arange(lag_count, dtype=np.int64) - lag_count // 2 + sample_count
    lag_angles = (bin_index[:, None] * lag_shift[None, :] % sample_count).astype(np.float32) * step
    lag_table = np.concatenate([np.cos(lag_angles), -np.sin(lag_angles)], 0).astype(ml_dtypes.bfloat16)
    return (jnp.asarray(dft_table), jnp.asarray(lag_table))


def whiten(spectrum, band_taper):
    bin_count = band_taper.shape[0]
    re_part = spectrum[..., :bin_count]
    im_part = spectrum[..., bin_count:]
    bin_power = re_part * re_part + im_part * im_part
    mean_power = jnp.mean(bin_power, axis=-1, keepdims=True)
    divisor = jnp.sqrt(bin_power + 0.5 * mean_power + 1e-06)
    gain_row = band_taper / divisor
    return jnp.concatenate([re_part * gain_row, im_part * gain_row], -1).astype(jnp.bfloat16)


def gather_over(piece, axis):
    count = lax.axis_size(axis)
    copies = jnp.broadcast_to(piece[None], (count,) + piece.shape)
    return lax.all_to_all(copies, axis, 0, 0, tiled=False)


def share_sources(picked):
    by_block = gather_over(picked, "chan")
    return gather_over(by_block, "tm")


def correlate_kernel(arr_ref, lag_ref, out_ref, src_sc, p_sc, q_sc, r_sc, stk_ref, *, norm, recv_off, src_off):
    segs, chans, bins = p_sc.shape
    n_src = src_sc.shape[1]
    block = out_ref.shape[0]
    step = pl.program_id(0)

    @pl.when(step == 0)
    def _():
        for g in range(segs):
            rec = arr_ref[g, recv_off : recv_off + chans, :].astype(jnp.float32)
            b_re, b_im = rec[:, :bins], rec[:, bins:]
            p_sc[g] = b_re
            q_sc[g] = -b_im - b_re
            r_sc[g] = b_re - b_im
            src_sc[g] = arr_ref[g, src_off : src_off + n_src, :].astype(jnp.float32)

    per_round = n_src // ROUNDS
    steps_per_round = per_round // block
    rnd = step // steps_per_round
    first_blk = (step % steps_per_round) * (block // SRC_BLK)

    def body(k, carry):
        acc = [[jnp.zeros((chans, bins), jnp.float32) for _ in range(3)] for _ in range(SRC_BLK)]
        base = (first_blk + k) * (ROUNDS * SRC_BLK) + rnd * SRC_BLK
        for g in range(segs):
            pg, qg, rg = p_sc[g], q_sc[g], r_sc[g]
            for u in range(SRC_BLK):
                row = src_sc[g, pl.ds(base + u, 1), :]
                a_re, a_im = row[:, :bins], row[:, bins:]
                acc[u][0] = acc[u][0] + pg * (a_re + a_im)
                acc[u][1] = acc[u][1] + qg * a_re
                acc[u][2] = acc[u][2] + rg * a_im
        for u in range(SRC_BLK):
            start = pl.multiple_of((k * SRC_BLK + u) * chans, chans)
            stk_ref[pl.ds(start, chans), :bins] = (acc[u][0] - acc[u][2]).astype(stk_ref.dtype)
            stk_ref[pl.ds(start, chans), bins:] = (acc[u][0] + acc[u][1]).astype(stk_ref.dtype)
        return carry

    lax.fori_loop(0, block // SRC_BLK, body, 0)
    lagged = jnp.dot(stk_ref[...], lag_ref[...], preferred_element_type=jnp.float32)
    out_ref[...] = (lagged * norm).astype(out_ref.dtype).reshape(out_ref.shape)


def correlate(arrived, recv_off, chans, src_off, n_src, lag_table, norm_scale, block=32):
    segs, _, feat = arrived.shape
    bins = feat // 2
    lags = lag_table.shape[1]
    return pl.pallas_call(
        functools.partial(correlate_kernel, norm=norm_scale, recv_off=recv_off, src_off=src_off),
        grid=(n_src // block,),
        in_specs=[
            pl.BlockSpec(arrived.shape, lambda i: (0, 0, 0)),
            pl.BlockSpec((feat, lags), lambda i: (0, 0)),
        ],
        out_specs=pl.BlockSpec((block, chans, lags), lambda i: (i, 0, 0)),
        out_shape=jax.ShapeDtypeStruct((n_src, chans, lags), jnp.bfloat16),
        scratch_shapes=[
            pltpu.VMEM((segs, n_src, feat), jnp.float32),
            pltpu.VMEM((segs, chans, bins), jnp.float32),
            pltpu.VMEM((segs, chans, bins), jnp.float32),
            pltpu.VMEM((segs, chans, bins), jnp.float32),
            pltpu.VMEM((block * chans, feat), jnp.bfloat16),
        ],
        compiler_params=pltpu.CompilerParams(
            dimension_semantics=("arbitrary",), vmem_limit_bytes=48 * 1024 * 1024
        ),
    )(arrived, lag_table)


def local(record, band_taper, src_offset):
    block_rows = record.shape[0]
    sample_count = record.shape[1]
    bin_count = band_taper.shape[0]
    dft_table, lag_table = const_tables(sample_count, bin_count, LOW_BIN, LAGS)
    spectrum = jnp.dot(record, dft_table, preferred_element_type=jnp.float32)
    whitened = whiten(spectrum, band_taper)
    chan_index = lax.axis_index("chan")
    offsets = lax.dynamic_slice_in_dim(src_offset, chan_index * SRC_BLK, SRC_BLK, 1)
    onehot = (offsets[:, :, None] == jnp.arange(block_rows, dtype=jnp.int32)[None, None, :]).astype(
        jnp.bfloat16
    )
    picked = jnp.einsum("rsb,bf->rsf", onehot, whitened, preferred_element_type=jnp.float32).astype(
        jnp.bfloat16
    )
    feat = picked.shape[-1]
    by_block = gather_over(picked.reshape(ROUNDS * SRC_BLK, feat), "chan")
    blocks = by_block.shape[0]
    tm_count = lax.axis_size("tm")
    to_send = jnp.concatenate(
        [
            whitened.reshape(tm_count, block_rows // tm_count, feat),
            jnp.broadcast_to(by_block.reshape(1, -1, feat), (tm_count, blocks * ROUNDS * SRC_BLK, feat)),
        ],
        1,
    )
    arrived = lax.all_to_all(to_send, "tm", 0, 0, tiled=False)
    chans = block_rows // tm_count
    n_src = blocks * ROUNDS * SRC_BLK
    norm_scale = 1.0 / math.sqrt(bin_count * tm_count)
    return correlate(arrived, 0, chans, chans, n_src, lag_table, norm_scale)


def solution(mesh):
    in_specs = (P("chan", "tm"), P(), P())
    out_specs = P(None, ("chan", "tm"), None)
    return jax.shard_map(local, mesh=mesh, in_specs=in_specs, out_specs=out_specs, check_vma=False)
```

```python
import functools
import math

import jax
import ml_dtypes
import numpy as np
import jax.numpy as jnp
from jax import lax
from jax.experimental import pallas as pl
from jax.experimental.pallas import tpu as pltpu
from jax.sharding import PartitionSpec as P

LOW_BIN = 32
LAGS = 256
SRC_BLK = 2
ROUNDS = 2


def make_tables(sample_count, bin_count, low_bin, lag_count):
    sample_index = jnp.arange(sample_count, dtype=jnp.int32)
    bin_index = low_bin + jnp.arange(bin_count, dtype=jnp.int32)
    angles = (sample_index[:, None] * bin_index[None, :] % sample_count).astype(jnp.float32) * (
        2.0 * math.pi / sample_count
    )
    dft_table = jnp.concatenate([jnp.cos(angles), -jnp.sin(angles)], 1).astype(jnp.bfloat16)
    lag_shift = jnp.arange(lag_count, dtype=jnp.int32) - lag_count // 2 + sample_count
    lag_angles = (bin_index[:, None] * lag_shift[None, :] % sample_count).astype(jnp.float32) * (
        2.0 * math.pi / sample_count
    )
    lag_table = jnp.concatenate([jnp.cos(lag_angles), -jnp.sin(lag_angles)], 0).astype(jnp.bfloat16)
    return (dft_table, lag_table)


def const_tables(sample_count, bin_count, low_bin, lag_count):
    sample_index = np.arange(sample_count, dtype=np.int64)
    bin_index = low_bin + np.arange(bin_count, dtype=np.int64)
    step = np.float32(2.0 * math.pi / sample_count)
    angles = (sample_index[:, None] * bin_index[None, :] % sample_count).astype(np.float32) * step
    dft_table = np.concatenate([np.cos(angles), -np.sin(angles)], 1).astype(ml_dtypes.bfloat16)
    lag_shift = np.arange(lag_count, dtype=np.int64) - lag_count // 2 + sample_count
    lag_angles = (bin_index[:, None] * lag_shift[None, :] % sample_count).astype(np.float32) * step
    lag_table = np.concatenate([np.cos(lag_angles), -np.sin(lag_angles)], 0).astype(ml_dtypes.bfloat16)
    return (jnp.asarray(dft_table), jnp.asarray(lag_table))


def whiten(spectrum, band_taper):
    bin_count = band_taper.shape[0]
    re_part = spectrum[..., :bin_count]
    im_part = spectrum[..., bin_count:]
    bin_power = re_part * re_part + im_part * im_part
    mean_power = jnp.mean(bin_power, axis=-1, keepdims=True)
    divisor = jnp.sqrt(bin_power + 0.5 * mean_power + 1e-06)
    gain_row = band_taper / divisor
    return jnp.concatenate([re_part * gain_row, im_part * gain_row], -1).astype(jnp.bfloat16)


def gather_over(piece, axis):
    count = lax.axis_size(axis)
    copies = jnp.broadcast_to(piece[None], (count,) + piece.shape)
    return lax.all_to_all(copies, axis, 0, 0, tiled=False)


def share_sources(picked):
    by_block = gather_over(picked, "chan")
    return gather_over(by_block, "tm")


def correlate_kernel(arr_ref, lag_ref, out_ref, src_sc, p_sc, q_sc, r_sc, stk_ref, *, norm, recv_off, src_off):
    segs, chans, bins = p_sc.shape
    n_src = src_sc.shape[1]
    block = out_ref.shape[0]
    step = pl.program_id(0)

    @pl.when(step == 0)
    def _():
        for g in range(segs):
            rec = arr_ref[g, recv_off : recv_off + chans, :].astype(jnp.float32)
            b_re, b_im = rec[:, :bins], rec[:, bins:]
            p_sc[g] = b_re
            q_sc[g] = -b_im - b_re
            r_sc[g] = b_re - b_im
            src_sc[g] = arr_ref[g, src_off : src_off + n_src, :].astype(jnp.float32)

    per_round = n_src // ROUNDS
    steps_per_round = per_round // block
    rnd = step // steps_per_round
    first_blk = (step % steps_per_round) * (block // SRC_BLK)

    group = stk_ref.shape[1] // chans
    n_groups = block // group
    pairs = group // SRC_BLK

    def products(q):
        slot = q % 2
        for pair in range(pairs):
            acc = [[jnp.zeros((chans, bins), jnp.float32) for _ in range(3)] for _ in range(SRC_BLK)]
            base = (first_blk + q * pairs + pair) * (ROUNDS * SRC_BLK) + rnd * SRC_BLK
            for g in range(segs):
                pg, qg, rg = p_sc[g], q_sc[g], r_sc[g]
                for u in range(SRC_BLK):
                    row = src_sc[g, pl.ds(base + u, 1), :]
                    a_re, a_im = row[:, :bins], row[:, bins:]
                    acc[u][0] = acc[u][0] + pg * (a_re + a_im)
                    acc[u][1] = acc[u][1] + qg * a_re
                    acc[u][2] = acc[u][2] + rg * a_im
            for u in range(SRC_BLK):
                rows = pl.ds((pair * SRC_BLK + u) * chans, chans)
                stk_ref[slot, rows, :bins] = (acc[u][0] - acc[u][2]).astype(stk_ref.dtype)
                stk_ref[slot, rows, bins:] = (acc[u][0] + acc[u][1]).astype(stk_ref.dtype)

    def lag_transform(q):
        lagged = jnp.dot(stk_ref[q % 2], lag_ref[...], preferred_element_type=jnp.float32)
        out_ref[pl.ds(q * group, group)] = (lagged * norm).astype(out_ref.dtype).reshape(group, chans, -1)

    products(0)

    def body(q, carry):
        lag_transform(q - 1)
        products(q)
        return carry

    lax.fori_loop(1, n_groups, body, 0)
    lag_transform(n_groups - 1)


def correlate(arrived, recv_off, chans, src_off, n_src, lag_table, norm_scale, block=32):
    segs, _, feat = arrived.shape
    bins = feat // 2
    lags = lag_table.shape[1]
    return pl.pallas_call(
        functools.partial(correlate_kernel, norm=norm_scale, recv_off=recv_off, src_off=src_off),
        grid=(n_src // block,),
        in_specs=[
            pl.BlockSpec(arrived.shape, lambda i: (0, 0, 0)),
            pl.BlockSpec((feat, lags), lambda i: (0, 0)),
        ],
        out_specs=pl.BlockSpec((block, chans, lags), lambda i: (i, 0, 0)),
        out_shape=jax.ShapeDtypeStruct((n_src, chans, lags), jnp.bfloat16),
        scratch_shapes=[
            pltpu.VMEM((segs, n_src, feat), jnp.float32),
            pltpu.VMEM((segs, chans, bins), jnp.float32),
            pltpu.VMEM((segs, chans, bins), jnp.float32),
            pltpu.VMEM((segs, chans, bins), jnp.float32),
            pltpu.VMEM((2, 8 * chans, feat), jnp.bfloat16),
        ],
        compiler_params=pltpu.CompilerParams(
            dimension_semantics=("arbitrary",), vmem_limit_bytes=48 * 1024 * 1024
        ),
    )(arrived, lag_table)


def local(record, band_taper, src_offset):
    block_rows = record.shape[0]
    sample_count = record.shape[1]
    bin_count = band_taper.shape[0]
    dft_table, lag_table = const_tables(sample_count, bin_count, LOW_BIN, LAGS)
    spectrum = jnp.dot(record, dft_table, preferred_element_type=jnp.float32)
    whitened = whiten(spectrum, band_taper)
    chan_index = lax.axis_index("chan")
    offsets = lax.dynamic_slice_in_dim(src_offset, chan_index * SRC_BLK, SRC_BLK, 1)
    onehot = (offsets[:, :, None] == jnp.arange(block_rows, dtype=jnp.int32)[None, None, :]).astype(
        jnp.bfloat16
    )
    picked = jnp.einsum("rsb,bf->rsf", onehot, whitened, preferred_element_type=jnp.float32).astype(
        jnp.bfloat16
    )
    feat = picked.shape[-1]
    by_block = gather_over(picked.reshape(ROUNDS * SRC_BLK, feat), "chan")
    blocks = by_block.shape[0]
    tm_count = lax.axis_size("tm")
    to_send = jnp.concatenate(
        [
            whitened.reshape(tm_count, block_rows // tm_count, feat),
            jnp.broadcast_to(by_block.reshape(1, -1, feat), (tm_count, blocks * ROUNDS * SRC_BLK, feat)),
        ],
        1,
    )
    arrived = lax.all_to_all(to_send, "tm", 0, 0, tiled=False)
    chans = block_rows // tm_count
    n_src = blocks * ROUNDS * SRC_BLK
    norm_scale = 1.0 / math.sqrt(bin_count * tm_count)
    return correlate(arrived, 0, chans, chans, n_src, lag_table, norm_scale)


def solution(mesh):
    in_specs = (P("chan", "tm"), P(), P())
    out_specs = P(None, ("chan", "tm"), None)
    return jax.shard_map(local, mesh=mesh, in_specs=in_specs, out_specs=out_specs, check_vma=False)
```
